256 devices in a mesh: grp: 4 (over y), dom: 64 (over x, z, core).
Axes of the slice: x: 4, y: 4, z: 8, core: 2. Of those that a mesh axis runs over, the one named last changes fastest.
Arguments:
- right_side: float32 [16, 524288], P(None, ('grp', 'dom')), may hold values from -38 to 38
- tile_values: float32 [24576, 128, 128], P(('grp', 'dom')), may hold values from 0 to 1, as said below
- tile_rows: int32 [24576], P(('grp', 'dom')), may hold values from 0 to 15
- tile_cols: int32 [24576], P(('grp', 'dom')), may hold values from 0 to 63, as said below
- tile_count: int32 [256], P(('grp', 'dom')), may hold values from 24 to 96, as said below
Outputs:
- solution_field: float32 [16, 524288], P(None, ('grp', 'dom'))
- residual: float32 [16, 524288], P(None, ('grp', 'dom'))
The draws below stay inside these ranges and needn't reach their ends.
Inputs may be any that keep to these rules, and one draw needn't show every extreme that they name: `tile_cols`: values w * 16 + j name block j of the device just below along dom (w = 0), of the device itself (w = 1), of the device just above along dom (w = 2), or of the device of the same dom index whose grp index differs in the lowest bit (w = 3). No slot of a device at the first dom index names w = 0, none at the last names w = 2. `tile_count`: some device has all 96 slots live. `tile_values`: each row of a tile has at least one nonzero entry.
All inputs are finite; a program needn't handle non-finite values.
Results may differ from the reference program's by a relative error of at most 0.0003.
Values sent between devices are 32-bit elements; how exact they have to be, the bound alone decides.
No kernel may reach another device: no remote copies, remote signals or barrier semaphores. Data moves between devices by JAX's collectives and lax.ppermute only.
A program may use at most 64 MiB of HBM per device.

```python
import jax
import jax.numpy as jnp
from jax import lax

Q = 16
TILE = 128
NBD = 16
TPD = 96
ITERS = 3
BLOCKS = 4096
POINTS = 524288
TILES = 24576
N_GRP = 4
N_DOM = 64


def draw_right_side(key, part):
    key_base = jax.random.fold_in(key, 11)
    key_one, key_two, key_three = jax.random.split(key_base, 3)
    position = jnp.arange(POINTS, dtype=jnp.float32) / POINTS
    along_axis = 3.0 ** (position - 0.5)
    point_factor = 10.0 ** (jax.random.uniform(key_two, (POINTS,), dtype=jnp.float32) - 0.5)
    column_factor = 3.0 ** (jax.random.uniform(key_three, (Q, 1), dtype=jnp.float32) - 0.5)
    base_values = jnp.clip(jax.random.normal(key_one, (Q, POINTS), dtype=jnp.float32), -4.0, 4.0)
    return (base_values * column_factor * along_axis[None, :] * point_factor[None, :]).astype(jnp.float32)


def draw_tile_values(key, part):
    key_base = jax.random.fold_in(key, 53)
    key_one, key_two, key_three, key_four = jax.random.split(key_base, 4)
    per_row = max(2, 32 * NBD // TPD)
    extra_share = max(per_row - 2, 0) / TILE
    columns = jnp.arange(TILE, dtype=jnp.int32)[None, None, :]
    first_pick = jax.random.randint(key_one, (TILES, TILE, 1), 0, TILE)
    second_pick = jax.random.randint(key_two, (TILES, TILE, 1), 0, TILE)
    further = jax.random.uniform(key_three, (TILES, TILE, TILE), dtype=jnp.float32) < extra_share
    kept = (columns == first_pick) | (columns == second_pick) | further
    distance = jax.random.uniform(key_four, (TILES, TILE, TILE), dtype=jnp.float32, minval=0.0, maxval=1.5)
    affinity = jnp.exp(-distance * distance)
    return jnp.where(kept, affinity, 0.0).astype(jnp.float32)


def draw_tile_cols(key, part):
    key_base = jax.random.fold_in(key, 23)
    key_one, key_two = jax.random.split(key_base)
    slots = jnp.arange(TILES, dtype=jnp.int32)
    device = slots // TPD
    dom_index = device % N_DOM
    picked = jax.random.randint(key_one, (TILES,), 0, 5)
    window = jnp.where(picked == 2, 0, jnp.where(picked == 3, 2, jnp.where(picked == 4, 3, 1)))
    window = jnp.where((window == 0) & (dom_index == 0), 1, window)
    window = jnp.where((window == 2) & (dom_index == N_DOM - 1), 1, window)
    within = jax.random.randint(key_two, (TILES,), 0, NBD)
    values = window * NBD + within
    values = jnp.where(slots == 0, 4 * NBD - 1, values)
    values = jnp.where(slots == TPD, 0, values)
    return values.astype(jnp.int32)


def draw_tile_count(key, part):
    key_base = jax.random.fold_in(key, 37)
    key_one, key_two, key_three, key_four = jax.random.split(key_base, 4)
    devices_all = N_GRP * N_DOM
    indices = jnp.arange(devices_all, dtype=jnp.int32)
    base_count = TPD // 4 + jax.random.randint(key_one, (devices_all,), 0, TPD // 4)
    hubs = jax.random.randint(key_two, (devices_all,), 0, 16) == 0
    chosen_high = jax.random.randint(key_three, (), 0, devices_all)
    chosen_low = (chosen_high + 1 + jax.random.randint(key_four, (), 0, devices_all - 1)) % devices_all
    counts = jnp.where(hubs | (indices == chosen_high), TPD, base_count)
    counts = jnp.where(indices == chosen_low, TPD // 4, counts)
    return counts.astype(jnp.int32)


def plant(array, key, smallest, top_value):
    extent = array.shape
    place = [jax.random.randint(jax.random.fold_in(key, axis), (), 0, extent[axis]) for axis in range(len(extent))]
    array = array.at[tuple(place)].set(smallest)
    longest = extent.index(max(extent))
    place[longest] = (place[longest] + 1) % extent[longest]
    return array.at[tuple(place)].set(top_value)


def setup_inputs(seed: int = 0) -> dict:
    streams_of = jax.random.split(jax.random.key(seed), 6)
    return {
        "right_side": draw_right_side(jax.random.fold_in(streams_of[5], 71), 0),
        "tile_values": draw_tile_values(jax.random.fold_in(streams_of[5], 71), 0),
        "tile_rows": plant(jax.random.randint(streams_of[2], (TILES,), 0, NBD), jax.random.fold_in(streams_of[2], 1), 0, NBD - 1).astype(jnp.int32),
        "tile_cols": draw_tile_cols(jax.random.fold_in(streams_of[5], 71), 0),
        "tile_count": draw_tile_count(jax.random.fold_in(streams_of[5], 71), 0),
    }


def tile_layout(tile_rows, tile_cols, tile_count):
    slots = jnp.arange(TILES, dtype=jnp.int32)
    device = slots // TPD
    grp_index = device // N_DOM
    dom_index = device % N_DOM
    live = slots % TPD < tile_count[device]
    row_global = device * NBD + tile_rows
    window = tile_cols // NBD
    within = tile_cols % NBD
    partner = jnp.bitwise_xor(grp_index, 1) * N_DOM + dom_index
    source = jnp.where(window == 0, device - 1, jnp.where(window == 1, device, jnp.where(window == 2, device + 1, partner)))
    col_global = (source * NBD + within).astype(jnp.int32)
    return (live, row_global.astype(jnp.int32), col_global)

def symmetric_product(tile_values, weight, row_global, col_global, field):
    blocks = field.reshape(Q, BLOCKS, TILE).transpose(1, 0, 2)
    forward = jnp.einsum('tij,tqj->tqi', tile_values, blocks[col_global], precision=lax.Precision.HIGHEST) * weight
    backward = jnp.einsum('tij,tqi->tqj', tile_values, blocks[row_global], precision=lax.Precision.HIGHEST) * weight
    total = jax.ops.segment_sum(forward, row_global, BLOCKS) + jax.ops.segment_sum(backward, col_global, BLOCKS)
    return total.transpose(1, 0, 2).reshape(Q, POINTS)

def reference(right_side, tile_values, tile_rows, tile_cols, tile_count):
    live, row_global, col_global = tile_layout(tile_rows, tile_cols, tile_count)
    weight = live.astype(tile_values.dtype)[:, None, None]
    row_terms = lax.optimization_barrier(jnp.sum(tile_values, axis=2)) * weight[:, :, 0]
    col_terms = lax.optimization_barrier(jnp.sum(tile_values, axis=1)) * weight[:, :, 0]
    degree = 1.0 + (jax.ops.segment_sum(row_terms, row_global, BLOCKS) + jax.ops.segment_sum(col_terms, col_global, BLOCKS)).reshape(POINTS)
    point_scale = 1.0 / jnp.sqrt(degree)

    def operator(field):
        return field - 0.8 * point_scale * symmetric_product(tile_values, weight, row_global, col_global, point_scale * field)
    solution_field = jnp.zeros_like(right_side)
    residual = right_side
    direction = right_side
    norm_now = lax.optimization_barrier(jnp.sum(residual * residual, axis=1))
    for iteration in range(ITERS):
        image = operator(direction)
        step_size = norm_now / lax.optimization_barrier(jnp.sum(direction * image, axis=1))
        solution_field = solution_field + step_size[:, None] * direction
        residual = residual - step_size[:, None] * image
        norm_next = lax.optimization_barrier(jnp.sum(residual * residual, axis=1))
        direction = residual + (norm_next / norm_now)[:, None] * direction
        norm_now = norm_next
    return (solution_field, residual)
```

```python
import jax
import jax.numpy as jnp
from jax import lax
from jax.sharding import PartitionSpec as P

TILE = 128
NBD = 16
ITERS = 3


batch_slots = 8
damping = 0.8


def with_halo(shard, sides, width):
    for axis, dim in sides:
        size, length = (lax.axis_size(axis), shard.shape[dim])
        up = [(i, (i + 1) % size) for i in range(size - 1)]
        down = [(j, i) for i, j in up]
        last = lax.slice_in_dim(shard, length - width, length, axis=dim)
        initial = lax.slice_in_dim(shard, 0, width, axis=dim)
        before = lax.ppermute(last, axis, up)
        after = lax.ppermute(initial, axis, down)
        shard = jnp.concatenate([before, shard, after], axis=dim)
    return shard


def partner_2(value, axis, stride):
    mask = 2**stride
    pairs = [(source, source ^ mask) for source in range(lax.axis_size(axis))]
    return lax.ppermute(value, axis, pairs)


def to_blocks(field):
    rows_here, points_here = field.shape
    return field.reshape(rows_here, points_here // TILE, TILE).transpose(1, 0, 2)


def from_blocks(blocks):
    return blocks.transpose(1, 0, 2).reshape(blocks.shape[1], blocks.shape[0] * blocks.shape[2])


def fetch_window(scaled):
    shard_width = scaled.shape[1]
    padded = with_halo(scaled, (("dom", 1),), shard_width)
    partner = partner_2(scaled, "grp", 0)
    return to_blocks(jnp.concatenate([padded, partner], axis=1))


def any_window(columns):
    return columns >= 0


def tile_pass(tiles, tile_rows, tile_cols, live_count, window_blocks, own_blocks, wanted):
    own_total = own_blocks.shape[0]
    window_total = window_blocks.shape[0]
    slot_total = tiles.shape[0]
    slot_ids = jnp.arange(slot_total, dtype=jnp.int32)
    active = ((slot_ids < live_count) & wanted(tile_cols)).astype(jnp.float32)
    forward = jnp.einsum(
        "bij,bqj->bqi", tiles, window_blocks[tile_cols], precision=lax.Precision.HIGHEST
    )
    backward = jnp.einsum(
        "bij,bqi->bqj", tiles, own_blocks[tile_rows], precision=lax.Precision.HIGHEST
    )
    row_pick = (tile_rows[:, None] == jnp.arange(own_total, dtype=jnp.int32)[None, :]).astype(
        jnp.float32
    ) * active[:, None]
    col_pick = (tile_cols[:, None] == jnp.arange(window_total, dtype=jnp.int32)[None, :]).astype(
        jnp.float32
    ) * active[:, None]
    row_sums = jnp.einsum("bn,bqi->nqi", row_pick, forward, precision=lax.Precision.HIGHEST)
    window_sums = jnp.einsum("bn,bqi->nqi", col_pick, backward, precision=lax.Precision.HIGHEST)
    return (row_sums, window_sums)


def return_sums(row_sums, window_sums):
    shard_blocks = row_sums.shape[0]
    own_part = from_blocks(row_sums + window_sums[shard_blocks : 2 * shard_blocks])
    sideways = jnp.concatenate(
        [
            from_blocks(window_sums[:shard_blocks]),
            from_blocks(window_sums[2 * shard_blocks : 3 * shard_blocks]),
        ],
        axis=1,
    )
    shard_width = own_part.shape[1]
    returned = with_halo(sideways, (("dom", 1),), shard_width)
    across = partner_2(from_blocks(window_sums[3 * shard_blocks :]), "grp", 0)
    return own_part + returned[:, :shard_width] + returned[:, 3 * shard_width :] + across


def degrees(tiles, tile_rows, tile_cols, live_count):
    slot_total = tiles.shape[0]
    active = (jnp.arange(slot_total, dtype=jnp.int32) < live_count).astype(jnp.float32)
    row_pick = (tile_rows[:, None] == jnp.arange(NBD, dtype=jnp.int32)[None, :]).astype(
        jnp.float32
    ) * active[:, None]
    col_pick = (tile_cols[:, None] == jnp.arange(4 * NBD, dtype=jnp.int32)[None, :]).astype(
        jnp.float32
    ) * active[:, None]
    row_sums = jnp.einsum(
        "tn,ti->ni", row_pick, jnp.sum(tiles, axis=2), precision=lax.Precision.HIGHEST
    )[:, None, :]
    window_sums = jnp.einsum(
        "tn,ti->ni", col_pick, jnp.sum(tiles, axis=1), precision=lax.Precision.HIGHEST
    )[:, None, :]
    return 1.0 + return_sums(row_sums, window_sums)[0]


def apply_operator(field, point_scale, tiles, tile_rows, tile_cols, live_count):
    scaled = point_scale * field
    own_blocks = to_blocks(scaled)
    row_sums, window_sums = tile_pass(
        tiles, tile_rows, tile_cols, live_count, fetch_window(scaled), own_blocks, any_window
    )
    return field - damping * point_scale * return_sums(row_sums, window_sums)


def squares(residual):
    return lax.psum(jnp.sum(residual * residual, axis=1), ("grp", "dom"))


def per_device(right_side, tile_values, tile_rows, tile_cols, tile_count):
    live_count = tile_count[0]
    point_scale = 1.0 / jnp.sqrt(degrees(tile_values, tile_rows, tile_cols, live_count))
    solution_field = jnp.zeros_like(right_side)
    residual = right_side
    direction = right_side
    norm_now = squares(residual)
    for iteration in range(ITERS):
        image = apply_operator(
            direction, point_scale, tile_values, tile_rows, tile_cols, live_count
        )
        curvature = lax.psum(jnp.sum(direction * image, axis=1), ("grp", "dom"))
        step_size = norm_now / curvature
        solution_field = solution_field + step_size[:, None] * direction
        residual = residual - step_size[:, None] * image
        norm_next = squares(residual)
        direction = residual + (norm_next / norm_now)[:, None] * direction
        norm_now = norm_next
    return (solution_field, residual)


def solution(mesh):
    placed = (
        P(None, ("grp", "dom")),
        P(("grp", "dom"), None, None),
        P(("grp", "dom")),
        P(("grp", "dom")),
        P(("grp", "dom")),
    )
    return jax.shard_map(
        per_device,
        mesh=mesh,
        in_specs=placed,
        out_specs=(P(None, ("grp", "dom")), P(None, ("grp", "dom"))),
        check_vma=False,
    )
```

```python
import jax
import jax.numpy as jnp
from jax import lax
from jax.sharding import PartitionSpec as P

TILE = 128
NBD = 16
ITERS = 3


batch_slots = 8
damping = 0.8


def with_halo(shard, sides, width):
    for axis, dim in sides:
        size, length = (lax.axis_size(axis), shard.shape[dim])
        up = [(i, (i + 1) % size) for i in range(size - 1)]
        down = [(j, i) for i, j in up]
        last = lax.slice_in_dim(shard, length - width, length, axis=dim)
        initial = lax.slice_in_dim(shard, 0, width, axis=dim)
        before = lax.ppermute(last, axis, up)
        after = lax.ppermute(initial, axis, down)
        shard = jnp.concatenate([before, shard, after], axis=dim)
    return shard


def partner_2(value, axis, stride):
    mask = 2**stride
    pairs = [(source, source ^ mask) for source in range(lax.axis_size(axis))]
    return lax.ppermute(value, axis, pairs)


def to_blocks(field):
    rows_here, points_here = field.shape
    return field.reshape(rows_here, points_here // TILE, TILE).transpose(1, 0, 2)


def from_blocks(blocks):
    return blocks.transpose(1, 0, 2).reshape(blocks.shape[1], blocks.shape[0] * blocks.shape[2])


def fetch_window(scaled):
    shard_width = scaled.shape[1]
    padded = with_halo(scaled, (("dom", 1),), shard_width)
    partner = partner_2(scaled, "grp", 0)
    return to_blocks(jnp.concatenate([padded, partner], axis=1))


def any_window(columns):
    return columns >= 0


def tile_pass(tiles, tile_rows, tile_cols, live_count, window_blocks, own_blocks, wanted):
    own_total = own_blocks.shape[0]
    window_total = window_blocks.shape[0]
    slot_total = tiles.shape[0]
    slot_ids = jnp.arange(slot_total, dtype=jnp.int32)
    active = ((slot_ids < live_count) & wanted(tile_cols)).astype(jnp.float32)
    forward = jnp.einsum(
        "bij,bqj->bqi", tiles, window_blocks[tile_cols], precision=lax.Precision.HIGHEST
    )
    backward = jnp.einsum(
        "bij,bqi->bqj", tiles, own_blocks[tile_rows], precision=lax.Precision.HIGHEST
    )
    row_pick = (tile_rows[:, None] == jnp.arange(own_total, dtype=jnp.int32)[None, :]).astype(
        jnp.float32
    ) * active[:, None]
    col_pick = (tile_cols[:, None] == jnp.arange(window_total, dtype=jnp.int32)[None, :]).astype(
        jnp.float32
    ) * active[:, None]
    row_sums = jnp.einsum("bn,bqi->nqi", row_pick, forward, precision=lax.Precision.HIGHEST)
    window_sums = jnp.einsum("bn,bqi->nqi", col_pick, backward, precision=lax.Precision.HIGHEST)
    return (row_sums, window_sums)


def return_sums(row_sums, window_sums):
    shard_blocks = row_sums.shape[0]
    own_part = from_blocks(row_sums + window_sums[shard_blocks : 2 * shard_blocks])
    sideways = jnp.concatenate(
        [
            from_blocks(window_sums[:shard_blocks]),
            from_blocks(window_sums[2 * shard_blocks : 3 * shard_blocks]),
        ],
        axis=1,
    )
    shard_width = own_part.shape[1]
    returned = with_halo(sideways, (("dom", 1),), shard_width)
    across = partner_2(from_blocks(window_sums[3 * shard_blocks :]), "grp", 0)
    return own_part + returned[:, :shard_width] + returned[:, 3 * shard_width :] + across


def degrees(tiles, tile_rows, tile_cols, live_count):
    slot_total = tiles.shape[0]
    active = (jnp.arange(slot_total, dtype=jnp.int32) < live_count).astype(jnp.float32)
    row_pick = (tile_rows[:, None] == jnp.arange(NBD, dtype=jnp.int32)[None, :]).astype(
        jnp.float32
    ) * active[:, None]
    col_pick = (tile_cols[:, None] == jnp.arange(4 * NBD, dtype=jnp.int32)[None, :]).astype(
        jnp.float32
    ) * active[:, None]
    row_sums = jnp.einsum(
        "tn,ti->ni", row_pick, jnp.sum(tiles, axis=2), precision=lax.Precision.HIGHEST
    )[:, None, :]
    window_sums = jnp.einsum(
        "tn,ti->ni", col_pick, jnp.sum(tiles, axis=1), precision=lax.Precision.HIGHEST
    )[:, None, :]
    return 1.0 + return_sums(row_sums, window_sums)[0]


def apply_operator(field, point_scale, tiles, tile_rows, tile_cols, live_count):
    scaled = point_scale * field
    own_blocks = to_blocks(scaled)
    row_sums, window_sums = tile_pass(
        tiles, tile_rows, tile_cols, live_count, fetch_window(scaled), own_blocks, any_window
    )
    return field - damping * point_scale * return_sums(row_sums, window_sums)


def xor_sum(value, axes):
    for axis in axes:
        size = lax.axis_size(axis)
        stride = 1
        while stride < size:
            masks = [0]
            for step in (stride, 2 * stride):
                if step < size:
                    masks = masks + [mask ^ step for mask in masks]
            parts = [value] + [
                lax.ppermute(value, axis, [(i, i ^ mask) for i in range(size)]) for mask in masks[1:]
            ]
            while len(parts) > 1:
                parts = [parts[k] + parts[k + 1] for k in range(0, len(parts), 2)]
            value = parts[0]
            stride *= 4
    return value


def total(value):
    return xor_sum(value, ("dom", "grp"))


def squares(residual):
    return total(jnp.sum(residual * residual, axis=1))


def per_device(right_side, tile_values, tile_rows, tile_cols, tile_count):
    live_count = tile_count[0]
    point_scale = 1.0 / jnp.sqrt(degrees(tile_values, tile_rows, tile_cols, live_count))
    solution_field = jnp.zeros_like(right_side)
    residual = right_side
    direction = right_side
    norm_now = squares(residual)
    for iteration in range(ITERS):
        image = apply_operator(
            direction, point_scale, tile_values, tile_rows, tile_cols, live_count
        )
        curvature = total(jnp.sum(direction * image, axis=1))
        step_size = norm_now / curvature
        solution_field = solution_field + step_size[:, None] * direction
        residual = residual - step_size[:, None] * image
        norm_next = squares(residual)
        direction = residual + (norm_next / norm_now)[:, None] * direction
        norm_now = norm_next
    return (solution_field, residual)


def solution(mesh):
    placed = (
        P(None, ("grp", "dom")),
        P(("grp", "dom"), None, None),
        P(("grp", "dom")),
        P(("grp", "dom")),
        P(("grp", "dom")),
    )
    return jax.shard_map(
        per_device,
        mesh=mesh,
        in_specs=placed,
        out_specs=(P(None, ("grp", "dom")), P(None, ("grp", "dom"))),
        check_vma=False,
    )
```

```python
import jax
import jax.numpy as jnp
from jax import lax
from jax.sharding import PartitionSpec as P

TILE = 128
NBD = 16
ITERS = 3


batch_slots = 8
damping = 0.8


def with_halo(shard, sides, width):
    for axis, dim in sides:
        size, length = (lax.axis_size(axis), shard.shape[dim])
        up = [(i, (i + 1) % size) for i in range(size - 1)]
        down = [(j, i) for i, j in up]
        last = lax.slice_in_dim(shard, length - width, length, axis=dim)
        initial = lax.slice_in_dim(shard, 0, width, axis=dim)
        before = lax.ppermute(last, axis, up)
        after = lax.ppermute(initial, axis, down)
        shard = jnp.concatenate([before, shard, after], axis=dim)
    return shard


def partner_2(value, axis, stride):
    mask = 2**stride
    pairs = [(source, source ^ mask) for source in range(lax.axis_size(axis))]
    return lax.ppermute(value, axis, pairs)


def to_blocks(field):
    rows_here, points_here = field.shape
    return field.reshape(rows_here, points_here // TILE, TILE).transpose(1, 0, 2)


def from_blocks(blocks):
    return blocks.transpose(1, 0, 2).reshape(blocks.shape[1], blocks.shape[0] * blocks.shape[2])


def fetch_window(scaled):
    shard_width = scaled.shape[1]
    padded = with_halo(scaled, (("dom", 1),), shard_width)
    partner = partner_2(scaled, "grp", 0)
    return to_blocks(jnp.concatenate([padded, partner], axis=1))


def any_window(columns):
    return columns >= 0


def tile_pass(tiles, tile_rows, tile_cols, live_count, window_blocks, own_blocks, wanted):
    own_total = own_blocks.shape[0]
    window_total = window_blocks.shape[0]
    slot_total = tiles.shape[0]
    slot_ids = jnp.arange(slot_total, dtype=jnp.int32)
    active = ((slot_ids < live_count) & wanted(tile_cols)).astype(jnp.float32)
    forward = jnp.einsum(
        "bij,bqj->bqi", tiles, window_blocks[tile_cols], precision=lax.Precision.HIGH
    )
    backward = jnp.einsum(
        "bij,bqi->bqj", tiles, own_blocks[tile_rows], precision=lax.Precision.HIGH
    )
    row_pick = (tile_rows[:, None] == jnp.arange(own_total, dtype=jnp.int32)[None, :]).astype(
        jnp.float32
    ) * active[:, None]
    col_pick = (tile_cols[:, None] == jnp.arange(window_total, dtype=jnp.int32)[None, :]).astype(
        jnp.float32
    ) * active[:, None]
    row_sums = jnp.einsum("bn,bqi->nqi", row_pick, forward, precision=lax.Precision.HIGHEST)
    window_sums = jnp.einsum("bn,bqi->nqi", col_pick, backward, precision=lax.Precision.HIGHEST)
    return (row_sums, window_sums)


def return_sums(row_sums, window_sums):
    shard_blocks = row_sums.shape[0]
    own_part = from_blocks(row_sums + window_sums[shard_blocks : 2 * shard_blocks])
    sideways = jnp.concatenate(
        [
            from_blocks(window_sums[:shard_blocks]),
            from_blocks(window_sums[2 * shard_blocks : 3 * shard_blocks]),
        ],
        axis=1,
    )
    shard_width = own_part.shape[1]
    returned = with_halo(sideways, (("dom", 1),), shard_width)
    across = partner_2(from_blocks(window_sums[3 * shard_blocks :]), "grp", 0)
    return own_part + returned[:, :shard_width] + returned[:, 3 * shard_width :] + across


def degrees(tiles, tile_rows, tile_cols, live_count):
    slot_total = tiles.shape[0]
    active = (jnp.arange(slot_total, dtype=jnp.int32) < live_count).astype(jnp.float32)
    row_pick = (tile_rows[:, None] == jnp.arange(NBD, dtype=jnp.int32)[None, :]).astype(
        jnp.float32
    ) * active[:, None]
    col_pick = (tile_cols[:, None] == jnp.arange(4 * NBD, dtype=jnp.int32)[None, :]).astype(
        jnp.float32
    ) * active[:, None]
    row_sums = jnp.einsum(
        "tn,ti->ni", row_pick, jnp.sum(tiles, axis=2), precision=lax.Precision.HIGHEST
    )[:, None, :]
    window_sums = jnp.einsum(
        "tn,ti->ni", col_pick, jnp.sum(tiles, axis=1), precision=lax.Precision.HIGHEST
    )[:, None, :]
    return 1.0 + return_sums(row_sums, window_sums)[0]


def apply_operator(field, point_scale, tiles, tile_rows, tile_cols, live_count):
    scaled = point_scale * field
    own_blocks = to_blocks(scaled)
    row_sums, window_sums = tile_pass(
        tiles, tile_rows, tile_cols, live_count, fetch_window(scaled), own_blocks, any_window
    )
    return field - damping * point_scale * return_sums(row_sums, window_sums)


def xor_sum(value, axes):
    for axis in axes:
        size = lax.axis_size(axis)
        stride = 1
        while stride < size:
            masks = [0]
            for step in (stride, 2 * stride):
                if step < size:
                    masks = masks + [mask ^ step for mask in masks]
            parts = [value] + [
                lax.ppermute(value, axis, [(i, i ^ mask) for i in range(size)]) for mask in masks[1:]
            ]
            while len(parts) > 1:
                parts = [parts[k] + parts[k + 1] for k in range(0, len(parts), 2)]
            value = parts[0]
            stride *= 4
    return value


def total(value):
    return xor_sum(value, ("dom", "grp"))


def squares(residual):
    return total(jnp.sum(residual * residual, axis=1))


def per_device(right_side, tile_values, tile_rows, tile_cols, tile_count):
    live_count = tile_count[0]
    point_scale = 1.0 / jnp.sqrt(degrees(tile_values, tile_rows, tile_cols, live_count))
    solution_field = jnp.zeros_like(right_side)
    residual = right_side
    direction = right_side
    norm_now = squares(residual)
    for iteration in range(ITERS):
        image = apply_operator(
            direction, point_scale, tile_values, tile_rows, tile_cols, live_count
        )
        curvature = total(jnp.sum(direction * image, axis=1))
        step_size = norm_now / curvature
        solution_field = solution_field + step_size[:, None] * direction
        residual = residual - step_size[:, None] * image
        norm_next = squares(residual)
        direction = residual + (norm_next / norm_now)[:, None] * direction
        norm_now = norm_next
    return (solution_field, residual)


def solution(mesh):
    placed = (
        P(None, ("grp", "dom")),
        P(("grp", "dom"), None, None),
        P(("grp", "dom")),
        P(("grp", "dom")),
        P(("grp", "dom")),
    )
    return jax.shard_map(
        per_device,
        mesh=mesh,
        in_specs=placed,
        out_specs=(P(None, ("grp", "dom")), P(None, ("grp", "dom"))),
        check_vma=False,
    )
```

```python
import jax
import jax.numpy as jnp
from jax import lax
from jax.sharding import PartitionSpec as P

TILE = 128
NBD = 16
ITERS = 3


batch_slots = 8
damping = 0.8


def with_halo(shard, sides, width):
    for axis, dim in sides:
        size, length = (lax.axis_size(axis), shard.shape[dim])
        up = [(i, (i + 1) % size) for i in range(size - 1)]
        down = [(j, i) for i, j in up]
        last = lax.slice_in_dim(shard, length - width, length, axis=dim)
        initial = lax.slice_in_dim(shard, 0, width, axis=dim)
        before = lax.ppermute(last, axis, up)
        after = lax.ppermute(initial, axis, down)
        shard = jnp.concatenate([before, shard, after], axis=dim)
    return shard


def partner_2(value, axis, stride):
    mask = 2**stride
    pairs = [(source, source ^ mask) for source in range(lax.axis_size(axis))]
    return lax.ppermute(value, axis, pairs)


def to_blocks(field):
    rows_here, points_here = field.shape
    return field.reshape(rows_here, points_here // TILE, TILE).transpose(1, 0, 2)


def from_blocks(blocks):
    return blocks.transpose(1, 0, 2).reshape(blocks.shape[1], blocks.shape[0] * blocks.shape[2])


def fetch_window(scaled):
    shard_width = scaled.shape[1]
    padded = with_halo(scaled, (("dom", 1),), shard_width)
    partner = partner_2(scaled, "grp", 0)
    return to_blocks(jnp.concatenate([padded, partner], axis=1))


def any_window(columns):
    return columns >= 0


def tile_pass(tiles, tile_rows, tile_cols, live_count, window_blocks, own_blocks, wanted):
    own_total = own_blocks.shape[0]
    window_total = window_blocks.shape[0]
    slot_total = tiles.shape[0]
    slot_ids = jnp.arange(slot_total, dtype=jnp.int32)
    active = ((slot_ids < live_count) & wanted(tile_cols)).astype(jnp.float32)
    forward = jnp.einsum(
        "bij,bqj->bqi", tiles, window_blocks[tile_cols], precision=lax.Precision.HIGH
    )
    backward = jnp.einsum(
        "bij,bqi->bqj", tiles, own_blocks[tile_rows], precision=lax.Precision.HIGH
    )
    row_pick = (tile_rows[:, None] == jnp.arange(own_total, dtype=jnp.int32)[None, :]).astype(
        jnp.float32
    ) * active[:, None]
    col_pick = (tile_cols[:, None] == jnp.arange(window_total, dtype=jnp.int32)[None, :]).astype(
        jnp.float32
    ) * active[:, None]
    row_sums = jnp.einsum("bn,bqi->nqi", row_pick, forward, precision=lax.Precision.HIGHEST)
    window_sums = jnp.einsum("bn,bqi->nqi", col_pick, backward, precision=lax.Precision.HIGHEST)
    return (row_sums, window_sums)


def return_sums(row_sums, window_sums):
    shard_blocks = row_sums.shape[0]
    own_part = from_blocks(row_sums + window_sums[shard_blocks : 2 * shard_blocks])
    sideways = jnp.concatenate(
        [
            from_blocks(window_sums[:shard_blocks]),
            from_blocks(window_sums[2 * shard_blocks : 3 * shard_blocks]),
        ],
        axis=1,
    )
    shard_width = own_part.shape[1]
    returned = with_halo(sideways, (("dom", 1),), shard_width)
    across = partner_2(from_blocks(window_sums[3 * shard_blocks :]), "grp", 0)
    return own_part + returned[:, :shard_width] + returned[:, 3 * shard_width :] + across


def degrees(tiles, tile_rows, tile_cols, live_count):
    slot_total = tiles.shape[0]
    active = (jnp.arange(slot_total, dtype=jnp.int32) < live_count).astype(jnp.float32)
    row_pick = (tile_rows[:, None] == jnp.arange(NBD, dtype=jnp.int32)[None, :]).astype(
        jnp.float32
    ) * active[:, None]
    col_pick = (tile_cols[:, None] == jnp.arange(4 * NBD, dtype=jnp.int32)[None, :]).astype(
        jnp.float32
    ) * active[:, None]
    row_sums = jnp.einsum(
        "tn,ti->ni", row_pick, jnp.sum(tiles, axis=2), precision=lax.Precision.HIGHEST
    )[:, None, :]
    window_sums = jnp.einsum(
        "tn,ti->ni", col_pick, jnp.sum(tiles, axis=1), precision=lax.Precision.HIGHEST
    )[:, None, :]
    return 1.0 + return_sums(row_sums, window_sums)[0]


def apply_operator(field, point_scale, tiles, tile_rows, tile_cols, live_count):
    scaled = point_scale * field
    own_blocks = to_blocks(scaled)
    row_sums, window_sums = tile_pass(
        tiles, tile_rows, tile_cols, live_count, fetch_window(scaled), own_blocks, any_window
    )
    return field - damping * point_scale * return_sums(row_sums, window_sums)


def xor_sum(value, axes):
    for axis in axes:
        size = lax.axis_size(axis)
        stride = 1
        while stride < size:
            masks = [0]
            for step in (stride, 2 * stride):
                if step < size:
                    masks = masks + [mask ^ step for mask in masks]
            parts = [value] + [
                lax.ppermute(value, axis, [(i, i ^ mask) for i in range(size)]) for mask in masks[1:]
            ]
            while len(parts) > 1:
                parts = [parts[k] + parts[k + 1] for k in range(0, len(parts), 2)]
            value = parts[0]
            stride *= 4
    return value


def total(value):
    return xor_sum(value, ("dom", "grp"))


def squares(residual):
    return total(jnp.sum(residual * residual, axis=1))


def per_device(right_side, tile_values, tile_rows, tile_cols, tile_count):
    live_count = tile_count[0]
    point_scale = 1.0 / jnp.sqrt(degrees(tile_values, tile_rows, tile_cols, live_count))
    solution_field = jnp.zeros_like(right_side)
    residual = right_side
    direction = right_side
    norm_now = squares(residual)
    image = apply_operator(direction, point_scale, tile_values, tile_rows, tile_cols, live_count)
    for iteration in range(ITERS):
        curvature = total(jnp.sum(direction * image, axis=1))
        step_size = norm_now / curvature
        solution_field = solution_field + step_size[:, None] * direction
        residual = residual - step_size[:, None] * image
        if iteration + 1 == ITERS:
            break
        norm_next = squares(residual)
        residual_image = apply_operator(
            residual, point_scale, tile_values, tile_rows, tile_cols, live_count
        )
        growth = (norm_next / norm_now)[:, None]
        direction = residual + growth * direction
        image = residual_image + growth * image
        norm_now = norm_next
    return (solution_field, residual)


def solution(mesh):
    placed = (
        P(None, ("grp", "dom")),
        P(("grp", "dom"), None, None),
        P(("grp", "dom")),
        P(("grp", "dom")),
        P(("grp", "dom")),
    )
    return jax.shard_map(
        per_device,
        mesh=mesh,
        in_specs=placed,
        out_specs=(P(None, ("grp", "dom")), P(None, ("grp", "dom"))),
        check_vma=False,
    )
```

```python
import jax
import jax.numpy as jnp
from jax import lax
from jax.sharding import PartitionSpec as P

TILE = 128
NBD = 16
ITERS = 3


batch_slots = 8
damping = 0.8


def with_halo(shard, sides, width):
    for axis, dim in sides:
        size, length = (lax.axis_size(axis), shard.shape[dim])
        up = [(i, (i + 1) % size) for i in range(size - 1)]
        down = [(j, i) for i, j in up]
        last = lax.slice_in_dim(shard, length - width, length, axis=dim)
        initial = lax.slice_in_dim(shard, 0, width, axis=dim)
        before = lax.ppermute(last, axis, up)
        after = lax.ppermute(initial, axis, down)
        shard = jnp.concatenate([before, shard, after], axis=dim)
    return shard


def partner_2(value, axis, stride):
    mask = 2**stride
    pairs = [(source, source ^ mask) for source in range(lax.axis_size(axis))]
    return lax.ppermute(value, axis, pairs)


def to_blocks(field):
    rows_here, points_here = field.shape
    return field.reshape(rows_here, points_here // TILE, TILE).transpose(1, 0, 2)


def from_blocks(blocks):
    return blocks.transpose(1, 0, 2).reshape(blocks.shape[1], blocks.shape[0] * blocks.shape[2])


def fetch_window(scaled):
    shard_width = scaled.shape[1]
    padded = with_halo(scaled, (("dom", 1),), shard_width)
    partner = partner_2(scaled, "grp", 0)
    return to_blocks(jnp.concatenate([padded, partner], axis=1))


def any_window(columns):
    return columns >= 0


def tile_pass(tiles, tile_rows, tile_cols, live_count, window_blocks, own_blocks, wanted):
    own_total = own_blocks.shape[0]
    window_total = window_blocks.shape[0]
    slot_total = tiles.shape[0]
    slot_ids = jnp.arange(slot_total, dtype=jnp.int32)
    active = ((slot_ids < live_count) & wanted(tile_cols)).astype(jnp.float32)
    forward = jnp.einsum(
        "bij,bqj->bqi", tiles, window_blocks[tile_cols], precision=lax.Precision.HIGH
    )
    backward = jnp.einsum(
        "bij,bqi->bqj", tiles, own_blocks[tile_rows], precision=lax.Precision.HIGH
    )
    row_pick = (tile_rows[:, None] == jnp.arange(own_total, dtype=jnp.int32)[None, :]).astype(
        jnp.float32
    ) * active[:, None]
    col_pick = (tile_cols[:, None] == jnp.arange(window_total, dtype=jnp.int32)[None, :]).astype(
        jnp.float32
    ) * active[:, None]
    row_sums = jnp.einsum("bn,bqi->nqi", row_pick, forward, precision=lax.Precision.HIGHEST)
    window_sums = jnp.einsum("bn,bqi->nqi", col_pick, backward, precision=lax.Precision.HIGHEST)
    return (row_sums, window_sums)


def return_sums(row_sums, window_sums):
    shard_blocks = row_sums.shape[0]
    own_part = from_blocks(row_sums + window_sums[shard_blocks : 2 * shard_blocks])
    sideways = jnp.concatenate(
        [
            from_blocks(window_sums[:shard_blocks]),
            from_blocks(window_sums[2 * shard_blocks : 3 * shard_blocks]),
        ],
        axis=1,
    )
    shard_width = own_part.shape[1]
    returned = with_halo(sideways, (("dom", 1),), shard_width)
    across = partner_2(from_blocks(window_sums[3 * shard_blocks :]), "grp", 0)
    return own_part + returned[:, :shard_width] + returned[:, 3 * shard_width :] + across


def degrees(tiles, tile_rows, tile_cols, live_count):
    slot_total = tiles.shape[0]
    active = (jnp.arange(slot_total, dtype=jnp.int32) < live_count).astype(jnp.float32)
    row_pick = (tile_rows[:, None] == jnp.arange(NBD, dtype=jnp.int32)[None, :]).astype(
        jnp.float32
    ) * active[:, None]
    col_pick = (tile_cols[:, None] == jnp.arange(4 * NBD, dtype=jnp.int32)[None, :]).astype(
        jnp.float32
    ) * active[:, None]
    row_sums = jnp.einsum(
        "tn,ti->ni", row_pick, jnp.sum(tiles, axis=2), precision=lax.Precision.HIGHEST
    )[:, None, :]
    window_sums = jnp.einsum(
        "tn,ti->ni", col_pick, jnp.sum(tiles, axis=1), precision=lax.Precision.HIGHEST
    )[:, None, :]
    return 1.0 + return_sums(row_sums, window_sums)[0]


def apply_operator(field, point_scale, tiles, tile_rows, tile_cols, live_count):
    scaled = point_scale * field
    own_blocks = to_blocks(scaled)
    row_sums, window_sums = tile_pass(
        tiles, tile_rows, tile_cols, live_count, fetch_window(scaled), own_blocks, any_window
    )
    return field - damping * point_scale * return_sums(row_sums, window_sums)


def xor_sum(value, axes):
    for axis in axes:
        size = lax.axis_size(axis)
        stride = 1
        while stride < size:
            masks = [0]
            for step in (stride, 2 * stride):
                if step < size:
                    masks = masks + [mask ^ step for mask in masks]
            parts = [value] + [
                lax.ppermute(value, axis, [(i, i ^ mask) for i in range(size)]) for mask in masks[1:]
            ]
            while len(parts) > 1:
                parts = [parts[k] + parts[k + 1] for k in range(0, len(parts), 2)]
            value = parts[0]
            stride *= 4
    return value


def total(value):
    return xor_sum(value, ("dom", "grp"))


def squares(residual):
    return total(jnp.sum(residual * residual, axis=1))


def per_device(right_side, tile_values, tile_rows, tile_cols, tile_count):
    live_count = tile_count[0]
    point_scale = 1.0 / jnp.sqrt(degrees(tile_values, tile_rows, tile_cols, live_count))
    solution_field = jnp.zeros_like(right_side)
    residual = right_side
    direction = right_side
    norm_now = None
    for iteration in range(ITERS):
        image = apply_operator(
            direction, point_scale, tile_values, tile_rows, tile_cols, live_count
        )
        if norm_now is None:
            both = total(
                jnp.stack([jnp.sum(direction * image, axis=1), jnp.sum(residual * residual, axis=1)])
            )
            curvature, norm_now = both[0], both[1]
        else:
            curvature = total(jnp.sum(direction * image, axis=1))
        step_size = norm_now / curvature
        solution_field = solution_field + step_size[:, None] * direction
        residual = residual - step_size[:, None] * image
        norm_next = squares(residual)
        direction = residual + (norm_next / norm_now)[:, None] * direction
        norm_now = norm_next
    return (solution_field, residual)


def solution(mesh):
    placed = (
        P(None, ("grp", "dom")),
        P(("grp", "dom"), None, None),
        P(("grp", "dom")),
        P(("grp", "dom")),
        P(("grp", "dom")),
    )
    return jax.shard_map(
        per_device,
        mesh=mesh,
        in_specs=placed,
        out_specs=(P(None, ("grp", "dom")), P(None, ("grp", "dom"))),
        check_vma=False,
    )
```

```python
import jax
import jax.numpy as jnp
from jax import lax
from jax.sharding import PartitionSpec as P

TILE = 128
NBD = 16
ITERS = 3


batch_slots = 8
damping = 0.8


def with_halo(shard, sides, width):
    for axis, dim in sides:
        size, length = (lax.axis_size(axis), shard.shape[dim])
        up = [(i, (i + 1) % size) for i in range(size - 1)]
        down = [(j, i) for i, j in up]
        last = lax.slice_in_dim(shard, length - width, length, axis=dim)
        initial = lax.slice_in_dim(shard, 0, width, axis=dim)
        before = lax.ppermute(last, axis, up)
        after = lax.ppermute(initial, axis, down)
        shard = jnp.concatenate([before, shard, after], axis=dim)
    return shard


def partner_2(value, axis, stride):
    mask = 2**stride
    pairs = [(source, source ^ mask) for source in range(lax.axis_size(axis))]
    return lax.ppermute(value, axis, pairs)


def to_blocks(field):
    rows_here, points_here = field.shape
    return field.reshape(rows_here, points_here // TILE, TILE).transpose(1, 0, 2)


def from_blocks(blocks):
    return blocks.transpose(1, 0, 2).reshape(blocks.shape[1], blocks.shape[0] * blocks.shape[2])


def fetch_window(scaled):
    shard_width = scaled.shape[1]
    padded = with_halo(scaled, (("dom", 1),), shard_width)
    partner = partner_2(scaled, "grp", 0)
    return to_blocks(jnp.concatenate([padded, partner], axis=1))


def any_window(columns):
    return columns >= 0


def tile_pass(tiles, tile_rows, tile_cols, live_count, window_blocks, own_blocks, wanted):
    own_total = own_blocks.shape[0]
    window_total = window_blocks.shape[0]
    slot_total = tiles.shape[0]
    slot_ids = jnp.arange(slot_total, dtype=jnp.int32)
    active = ((slot_ids < live_count) & wanted(tile_cols)).astype(jnp.float32)
    forward = jnp.einsum(
        "bij,bqj->bqi", tiles, window_blocks[tile_cols], precision=lax.Precision.HIGH
    )
    backward = jnp.einsum(
        "bij,bqi->bqj", tiles, own_blocks[tile_rows], precision=lax.Precision.HIGH
    )
    row_pick = (tile_rows[:, None] == jnp.arange(own_total, dtype=jnp.int32)[None, :]).astype(
        jnp.float32
    ) * active[:, None]
    col_pick = (tile_cols[:, None] == jnp.arange(window_total, dtype=jnp.int32)[None, :]).astype(
        jnp.float32
    ) * active[:, None]
    row_sums = jnp.einsum("bn,bqi->nqi", row_pick, forward, precision=lax.Precision.HIGHEST)
    window_sums = jnp.einsum("bn,bqi->nqi", col_pick, backward, precision=lax.Precision.HIGHEST)
    return (row_sums, window_sums)


def return_sums(row_sums, window_sums):
    shard_blocks = row_sums.shape[0]
    own_part = from_blocks(row_sums + window_sums[shard_blocks : 2 * shard_blocks])
    sideways = jnp.concatenate(
        [
            from_blocks(window_sums[:shard_blocks]),
            from_blocks(window_sums[2 * shard_blocks : 3 * shard_blocks]),
        ],
        axis=1,
    )
    shard_width = own_part.shape[1]
    returned = with_halo(sideways, (("dom", 1),), shard_width)
    across = partner_2(from_blocks(window_sums[3 * shard_blocks :]), "grp", 0)
    return own_part + returned[:, :shard_width] + returned[:, 3 * shard_width :] + across


def degrees(tiles, tile_rows, tile_cols, live_count):
    slot_total = tiles.shape[0]
    active = (jnp.arange(slot_total, dtype=jnp.int32) < live_count).astype(jnp.float32)
    row_pick = (tile_rows[:, None] == jnp.arange(NBD, dtype=jnp.int32)[None, :]).astype(
        jnp.float32
    ) * active[:, None]
    col_pick = (tile_cols[:, None] == jnp.arange(4 * NBD, dtype=jnp.int32)[None, :]).astype(
        jnp.float32
    ) * active[:, None]
    row_sums = jnp.einsum(
        "tn,ti->ni", row_pick, jnp.sum(tiles, axis=2), precision=lax.Precision.HIGHEST
    )[:, None, :]
    window_sums = jnp.einsum(
        "tn,ti->ni", col_pick, jnp.sum(tiles, axis=1), precision=lax.Precision.HIGHEST
    )[:, None, :]
    return 1.0 + return_sums(row_sums, window_sums)[0]


def apply_operator(field, point_scale, tiles, tile_rows, tile_cols, live_count):
    scaled = point_scale * field
    own_blocks = to_blocks(scaled)
    row_sums, window_sums = tile_pass(
        tiles, tile_rows, tile_cols, live_count, fetch_window(scaled), own_blocks, any_window
    )
    return field - damping * point_scale * return_sums(row_sums, window_sums)


def apply_with_curvature(field, point_scale, tiles, tile_rows, tile_cols, live_count):
    scaled = point_scale * field
    own_blocks = to_blocks(scaled)
    row_sums, window_sums = tile_pass(
        tiles, tile_rows, tile_cols, live_count, fetch_window(scaled), own_blocks, any_window
    )
    bend = jnp.sum(own_blocks * row_sums, axis=(0, 2))
    curvature = jnp.sum(field * field, axis=1) - 2.0 * damping * bend
    image = field - damping * point_scale * return_sums(row_sums, window_sums)
    return (image, curvature)


def xor_sum(value, axes):
    for axis in axes:
        size = lax.axis_size(axis)
        stride = 1
        while stride < size:
            masks = [0]
            for step in (stride, 2 * stride):
                if step < size:
                    masks = masks + [mask ^ step for mask in masks]
            parts = [value] + [
                lax.ppermute(value, axis, [(i, i ^ mask) for i in range(size)]) for mask in masks[1:]
            ]
            while len(parts) > 1:
                parts = [parts[k] + parts[k + 1] for k in range(0, len(parts), 2)]
            value = parts[0]
            stride *= 4
    return value


def total(value):
    return xor_sum(value, ("dom", "grp"))


def squares(residual):
    return total(jnp.sum(residual * residual, axis=1))


def per_device(right_side, tile_values, tile_rows, tile_cols, tile_count):
    live_count = tile_count[0]
    point_scale = 1.0 / jnp.sqrt(degrees(tile_values, tile_rows, tile_cols, live_count))
    solution_field = jnp.zeros_like(right_side)
    residual = right_side
    direction = right_side
    norm_now = None
    for iteration in range(ITERS):
        image, bent = apply_with_curvature(
            direction, point_scale, tile_values, tile_rows, tile_cols, live_count
        )
        if norm_now is None:
            both = total(jnp.stack([bent, jnp.sum(residual * residual, axis=1)]))
            curvature, norm_now = both[0], both[1]
        else:
            curvature = total(bent)
        step_size = norm_now / curvature
        solution_field = solution_field + step_size[:, None] * direction
        residual = residual - step_size[:, None] * image
        norm_next = squares(residual)
        direction = residual + (norm_next / norm_now)[:, None] * direction
        norm_now = norm_next
    return (solution_field, residual)


def solution(mesh):
    placed = (
        P(None, ("grp", "dom")),
        P(("grp", "dom"), None, None),
        P(("grp", "dom")),
        P(("grp", "dom")),
        P(("grp", "dom")),
    )
    return jax.shard_map(
        per_device,
        mesh=mesh,
        in_specs=placed,
        out_specs=(P(None, ("grp", "dom")), P(None, ("grp", "dom"))),
        check_vma=False,
    )
```

```python
import jax
import jax.numpy as jnp
from jax import lax
from jax.sharding import PartitionSpec as P

TILE = 128
NBD = 16
ITERS = 3


batch_slots = 8
damping = 0.8


def with_halo(shard, sides, width):
    for axis, dim in sides:
        size, length = (lax.axis_size(axis), shard.shape[dim])
        up = [(i, (i + 1) % size) for i in range(size - 1)]
        down = [(j, i) for i, j in up]
        last = lax.slice_in_dim(shard, length - width, length, axis=dim)
        initial = lax.slice_in_dim(shard, 0, width, axis=dim)
        before = lax.ppermute(last, axis, up)
        after = lax.ppermute(initial, axis, down)
        shard = jnp.concatenate([before, shard, after], axis=dim)
    return shard


def partner_2(value, axis, stride):
    mask = 2**stride
    pairs = [(source, source ^ mask) for source in range(lax.axis_size(axis))]
    return lax.ppermute(value, axis, pairs)


def to_blocks(field):
    rows_here, points_here = field.shape
    return field.reshape(rows_here, points_here // TILE, TILE).transpose(1, 0, 2)


def from_blocks(blocks):
    return blocks.transpose(1, 0, 2).reshape(blocks.shape[1], blocks.shape[0] * blocks.shape[2])


def fetch_window(scaled):
    shard_width = scaled.shape[1]
    padded = with_halo(scaled, (("dom", 1),), shard_width)
    partner = partner_2(scaled, "grp", 0)
    return to_blocks(jnp.concatenate([padded, partner], axis=1))


def any_window(columns):
    return columns >= 0


def tile_pass(tiles, tile_rows, tile_cols, live_count, window_blocks, own_blocks, wanted):
    own_total = own_blocks.shape[0]
    window_total = window_blocks.shape[0]
    slot_total = tiles.shape[0]
    slot_ids = jnp.arange(slot_total, dtype=jnp.int32)
    active = ((slot_ids < live_count) & wanted(tile_cols)).astype(jnp.float32)
    forward = jnp.einsum(
        "bij,bqj->bqi", tiles, window_blocks[tile_cols], precision=lax.Precision.HIGH
    )
    backward = jnp.einsum(
        "bij,bqi->bqj", tiles, own_blocks[tile_rows], precision=lax.Precision.HIGH
    )
    row_pick = (tile_rows[:, None] == jnp.arange(own_total, dtype=jnp.int32)[None, :]).astype(
        jnp.float32
    ) * active[:, None]
    col_pick = (tile_cols[:, None] == jnp.arange(window_total, dtype=jnp.int32)[None, :]).astype(
        jnp.float32
    ) * active[:, None]
    row_sums = jnp.einsum("bn,bqi->nqi", row_pick, forward, precision=lax.Precision.HIGH)
    window_sums = jnp.einsum("bn,bqi->nqi", col_pick, backward, precision=lax.Precision.HIGH)
    return (row_sums, window_sums)


def return_sums(row_sums, window_sums):
    shard_blocks = row_sums.shape[0]
    own_part = from_blocks(row_sums + window_sums[shard_blocks : 2 * shard_blocks])
    sideways = jnp.concatenate(
        [
            from_blocks(window_sums[:shard_blocks]),
            from_blocks(window_sums[2 * shard_blocks : 3 * shard_blocks]),
        ],
        axis=1,
    )
    shard_width = own_part.shape[1]
    returned = with_halo(sideways, (("dom", 1),), shard_width)
    across = partner_2(from_blocks(window_sums[3 * shard_blocks :]), "grp", 0)
    return own_part + returned[:, :shard_width] + returned[:, 3 * shard_width :] + across


def degrees(tiles, tile_rows, tile_cols, live_count):
    slot_total = tiles.shape[0]
    active = (jnp.arange(slot_total, dtype=jnp.int32) < live_count).astype(jnp.float32)
    row_pick = (tile_rows[:, None] == jnp.arange(NBD, dtype=jnp.int32)[None, :]).astype(
        jnp.float32
    ) * active[:, None]
    col_pick = (tile_cols[:, None] == jnp.arange(4 * NBD, dtype=jnp.int32)[None, :]).astype(
        jnp.float32
    ) * active[:, None]
    row_sums = jnp.einsum(
        "tn,ti->ni", row_pick, jnp.sum(tiles, axis=2), precision=lax.Precision.HIGHEST
    )[:, None, :]
    window_sums = jnp.einsum(
        "tn,ti->ni", col_pick, jnp.sum(tiles, axis=1), precision=lax.Precision.HIGHEST
    )[:, None, :]
    return 1.0 + return_sums(row_sums, window_sums)[0]


def apply_operator(field, point_scale, tiles, tile_rows, tile_cols, live_count):
    scaled = point_scale * field
    own_blocks = to_blocks(scaled)
    row_sums, window_sums = tile_pass(
        tiles, tile_rows, tile_cols, live_count, fetch_window(scaled), own_blocks, any_window
    )
    return field - damping * point_scale * return_sums(row_sums, window_sums)


def xor_sum(value, axes):
    for axis in axes:
        size = lax.axis_size(axis)
        stride = 1
        while stride < size:
            masks = [0]
            for step in (stride, 2 * stride):
                if step < size:
                    masks = masks + [mask ^ step for mask in masks]
            parts = [value] + [
                lax.ppermute(value, axis, [(i, i ^ mask) for i in range(size)]) for mask in masks[1:]
            ]
            while len(parts) > 1:
                parts = [parts[k] + parts[k + 1] for k in range(0, len(parts), 2)]
            value = parts[0]
            stride *= 4
    return value


def total(value):
    return xor_sum(value, ("dom", "grp"))


def squares(residual):
    return total(jnp.sum(residual * residual, axis=1))


def per_device(right_side, tile_values, tile_rows, tile_cols, tile_count):
    live_count = tile_count[0]
    point_scale = 1.0 / jnp.sqrt(degrees(tile_values, tile_rows, tile_cols, live_count))
    solution_field = jnp.zeros_like(right_side)
    residual = right_side
    direction = right_side
    norm_now = None
    for iteration in range(ITERS):
        image = apply_operator(
            direction, point_scale, tile_values, tile_rows, tile_cols, live_count
        )
        if norm_now is None:
            both = total(
                jnp.stack([jnp.sum(direction * image, axis=1), jnp.sum(residual * residual, axis=1)])
            )
            curvature, norm_now = both[0], both[1]
        else:
            curvature = total(jnp.sum(direction * image, axis=1))
        step_size = norm_now / curvature
        solution_field = solution_field + step_size[:, None] * direction
        residual = residual - step_size[:, None] * image
        norm_next = squares(residual)
        direction = residual + (norm_next / norm_now)[:, None] * direction
        norm_now = norm_next
    return (solution_field, residual)


def solution(mesh):
    placed = (
        P(None, ("grp", "dom")),
        P(("grp", "dom"), None, None),
        P(("grp", "dom")),
        P(("grp", "dom")),
        P(("grp", "dom")),
    )
    return jax.shard_map(
        per_device,
        mesh=mesh,
        in_specs=placed,
        out_specs=(P(None, ("grp", "dom")), P(None, ("grp", "dom"))),
        check_vma=False,
    )
```

```python
import jax
import jax.numpy as jnp
from jax import lax
from jax.sharding import PartitionSpec as P

TILE = 128
NBD = 16
ITERS = 3


batch_slots = 8
damping = 0.8


def with_halo(shard, sides, width):
    for axis, dim in sides:
        size, length = (lax.axis_size(axis), shard.shape[dim])
        up = [(i, (i + 1) % size) for i in range(size - 1)]
        down = [(j, i) for i, j in up]
        last = lax.slice_in_dim(shard, length - width, length, axis=dim)
        initial = lax.slice_in_dim(shard, 0, width, axis=dim)
        before = lax.ppermute(last, axis, up)
        after = lax.ppermute(initial, axis, down)
        shard = jnp.concatenate([before, shard, after], axis=dim)
    return shard


def partner_2(value, axis, stride):
    mask = 2**stride
    pairs = [(source, source ^ mask) for source in range(lax.axis_size(axis))]
    return lax.ppermute(value, axis, pairs)


def to_blocks(field):
    rows_here, points_here = field.shape
    return field.reshape(rows_here, points_here // TILE, TILE).transpose(1, 0, 2)


def from_blocks(blocks):
    return blocks.transpose(1, 0, 2).reshape(blocks.shape[1], blocks.shape[0] * blocks.shape[2])


def fetch_window(scaled):
    shard_width = scaled.shape[1]
    padded = with_halo(scaled, (("dom", 1),), shard_width)
    partner = partner_2(scaled, "grp", 0)
    return to_blocks(jnp.concatenate([padded, partner], axis=1))


def any_window(columns):
    return columns >= 0


def tile_pass(tiles, tile_rows, tile_cols, live_count, window_blocks, own_blocks, wanted):
    own_total = own_blocks.shape[0]
    window_total = window_blocks.shape[0]
    slot_total = tiles.shape[0]
    slot_ids = jnp.arange(slot_total, dtype=jnp.int32)
    active = ((slot_ids < live_count) & wanted(tile_cols)).astype(jnp.float32)
    forward = jnp.einsum(
        "bij,bqj->bqi", tiles, window_blocks[tile_cols], precision=lax.Precision.HIGH
    )
    backward = jnp.einsum(
        "bij,bqi->bqj", tiles, own_blocks[tile_rows], precision=lax.Precision.HIGH
    )
    row_pick = (tile_rows[:, None] == jnp.arange(own_total, dtype=jnp.int32)[None, :]).astype(
        jnp.float32
    ) * active[:, None]
    col_pick = (tile_cols[:, None] == jnp.arange(window_total, dtype=jnp.int32)[None, :]).astype(
        jnp.float32
    ) * active[:, None]
    row_sums = jnp.einsum("bn,bqi->nqi", row_pick, forward, precision=lax.Precision.HIGH)
    window_sums = jnp.einsum("bn,bqi->nqi", col_pick, backward, precision=lax.Precision.HIGH)
    return (row_sums, window_sums)


def return_sums(row_sums, window_sums):
    shard_blocks = row_sums.shape[0]
    own_part = from_blocks(row_sums + window_sums[shard_blocks : 2 * shard_blocks])
    sideways = jnp.concatenate(
        [
            from_blocks(window_sums[:shard_blocks]),
            from_blocks(window_sums[2 * shard_blocks : 3 * shard_blocks]),
        ],
        axis=1,
    )
    shard_width = own_part.shape[1]
    returned = with_halo(sideways, (("dom", 1),), shard_width)
    across = partner_2(from_blocks(window_sums[3 * shard_blocks :]), "grp", 0)
    return own_part + returned[:, :shard_width] + returned[:, 3 * shard_width :] + across


def degrees(tiles, tile_rows, tile_cols, live_count):
    slot_total = tiles.shape[0]
    active = (jnp.arange(slot_total, dtype=jnp.int32) < live_count).astype(jnp.float32)
    row_pick = (tile_rows[:, None] == jnp.arange(NBD, dtype=jnp.int32)[None, :]).astype(
        jnp.float32
    ) * active[:, None]
    col_pick = (tile_cols[:, None] == jnp.arange(4 * NBD, dtype=jnp.int32)[None, :]).astype(
        jnp.float32
    ) * active[:, None]
    row_sums = jnp.einsum(
        "tn,ti->ni", row_pick, jnp.sum(tiles, axis=2), precision=lax.Precision.HIGH
    )[:, None, :]
    window_sums = jnp.einsum(
        "tn,ti->ni", col_pick, jnp.sum(tiles, axis=1), precision=lax.Precision.HIGH
    )[:, None, :]
    return 1.0 + return_sums(row_sums, window_sums)[0]


def apply_operator(field, point_scale, tiles, tile_rows, tile_cols, live_count):
    scaled = point_scale * field
    own_blocks = to_blocks(scaled)
    row_sums, window_sums = tile_pass(
        tiles, tile_rows, tile_cols, live_count, fetch_window(scaled), own_blocks, any_window
    )
    return field - damping * point_scale * return_sums(row_sums, window_sums)


def xor_sum(value, axes):
    for axis in axes:
        size = lax.axis_size(axis)
        stride = 1
        while stride < size:
            masks = [0]
            for step in (stride, 2 * stride):
                if step < size:
                    masks = masks + [mask ^ step for mask in masks]
            parts = [value] + [
                lax.ppermute(value, axis, [(i, i ^ mask) for i in range(size)]) for mask in masks[1:]
            ]
            while len(parts) > 1:
                parts = [parts[k] + parts[k + 1] for k in range(0, len(parts), 2)]
            value = parts[0]
            stride *= 4
    return value


def total(value):
    return xor_sum(value, ("dom", "grp"))


def squares(residual):
    return total(jnp.sum(residual * residual, axis=1))


def per_device(right_side, tile_values, tile_rows, tile_cols, tile_count):
    live_count = tile_count[0]
    point_scale = 1.0 / jnp.sqrt(degrees(tile_values, tile_rows, tile_cols, live_count))
    solution_field = jnp.zeros_like(right_side)
    residual = right_side
    direction = right_side
    norm_now = None
    for iteration in range(ITERS):
        image = apply_operator(
            direction, point_scale, tile_values, tile_rows, tile_cols, live_count
        )
        if norm_now is None:
            both = total(
                jnp.stack([jnp.sum(direction * image, axis=1), jnp.sum(residual * residual, axis=1)])
            )
            curvature, norm_now = both[0], both[1]
        else:
            curvature = total(jnp.sum(direction * image, axis=1))
        step_size = norm_now / curvature
        solution_field = solution_field + step_size[:, None] * direction
        residual = residual - step_size[:, None] * image
        norm_next = squares(residual)
        direction = residual + (norm_next / norm_now)[:, None] * direction
        norm_now = norm_next
    return (solution_field, residual)


def solution(mesh):
    placed = (
        P(None, ("grp", "dom")),
        P(("grp", "dom"), None, None),
        P(("grp", "dom")),
        P(("grp", "dom")),
        P(("grp", "dom")),
    )
    return jax.shard_map(
        per_device,
        mesh=mesh,
        in_specs=placed,
        out_specs=(P(None, ("grp", "dom")), P(None, ("grp", "dom"))),
        check_vma=False,
    )
```
